256 devices in a mesh: prow: 8 (over z_hi, core), pcol: 32 (over x, z_lo, y).
Axes of the slice: x: 4, y: 4, z: 8 (z_hi: 4, z_lo: 2; z = z_hi * 2 + z_lo), core: 2. Of those that a mesh axis runs over, the one named last changes fastest.
Arguments:
- slab: float32 [2048, 98304], P('pcol', 'prow'), may hold values from -6 to 6
- vectors: float32 [98304, 512], P(('prow', 'pcol')), may hold values from -0.01953125 to 0.01953125
- tfactors: float32 [4, 128, 128], replicated, as said below
Outputs:
- transformed: float32 [2048, 98304], P('pcol', 'prow')
The draws below stay inside these ranges and needn't reach their ends.
Inputs may be any that keep to these rules, and one draw needn't show every extreme that they name: Each tfactors[k] is upper triangular with diagonal entries between 1 and 2.
All inputs are finite; a program needn't handle non-finite values.
Results may differ from the reference program's by a relative error of at most 0.0001.
Values sent between devices are 32-bit elements; how exact they have to be, the bound alone decides.
No kernel may reach another device: no remote copies, remote signals or barrier semaphores. Data moves between devices by JAX's collectives and lax.ppermute only.
A program may use at most 128 MiB of HBM per device.

```python
import jax
import jax.numpy as jnp
from jax import lax

N = 98304
NB = 128
NBLK = 4
M = 2048


def draw_tfactors(key, part):
    key_diag, key_off = jax.random.split(key)
    diag_vals = jax.random.uniform(key_diag, (NBLK, NB), jnp.float32, 1.0, 2.0)
    off_vals = jax.random.normal(key_off, (NBLK, NB, NB), jnp.float32) * (0.5 * NB ** (-0.5))
    upper = jnp.triu(off_vals, 1)
    return upper + diag_vals[:, :, None] * jnp.eye(NB, dtype=jnp.float32)[None, :, :]


def steps_of(own_key, dims, shards, least, top_value):
    loudness = 1.0
    for position, shards_of in shards:
        draws = jax.random.uniform(jax.random.fold_in(jax.random.fold_in(own_key, 6), position), (shards_of,), jnp.float32, least / len(shards), top_value / len(shards))
        loudness = loudness * jnp.repeat(jnp.exp(draws), dims[position] // shards_of).reshape((-1,) + (1,) * (len(dims) - 1 - position))
    return loudness


def bell_draw(key, shape, spread, bound, cuts=(), held_as=jnp.bfloat16):
    result = jax.random.normal(key, shape, jnp.float32) * spread
    if len(cuts) > 0:
        result = steps_of(key, shape, cuts, -0.22, 0.18) * result
    return jnp.clip(result, min=-bound, max=bound).astype(held_as)


def setup_inputs(seed: int = 0) -> dict:
    splits = jax.random.split(jax.random.key(seed), 4)
    return {
        "slab": bell_draw(splits[0], (M, N), 1.0, 6.0, ((0, 32), (1, 8)), jnp.float32),
        "vectors": bell_draw(splits[1], (N, NB * NBLK), N ** -0.5, 0.01953125, ((0, 256),), jnp.float32),
        "tfactors": draw_tfactors(jax.random.fold_in(splits[3], 71), 0),
    }


def reference(slab, vectors, tfactors):
    transformed = slab
    for k in reversed(range(NBLK)):
        block = vectors[:, k * NB:(k + 1) * NB]
        part = jnp.dot(transformed, block, precision=lax.Precision.HIGHEST, preferred_element_type=jnp.float32)
        scaled = jnp.dot(part, tfactors[k].T, precision=lax.Precision.HIGHEST, preferred_element_type=jnp.float32)
        transformed = transformed - jnp.dot(scaled, block.T, precision=lax.Precision.HIGHEST, preferred_element_type=jnp.float32)
    return transformed
```

```python
import jax
import jax.numpy as jnp
from jax import lax
from jax.sharding import Mesh
from jax.sharding import PartitionSpec as P

PCOL_PARTS = (4, 2, 4)
GROUP = ("zl", "y")


def matmul(left, right):
    return jnp.dot(left, right, precision=lax.Precision.HIGHEST, preferred_element_type=jnp.float32)


def per_device(slab, vectors, tfactors):
    rows, cols = slab.shape
    depth = vectors.shape[0]
    count = tfactors.shape[0]
    width = tfactors.shape[1]
    nx = PCOL_PARTS[0]
    ng = PCOL_PARTS[1] * PCOL_PARTS[2]

    gram = lax.psum(matmul(vectors[:, width:].T, vectors[:, : (count - 1) * width]), ("prow", "x", "zl", "y"))

    basis = lax.all_gather(vectors, "x", axis=0, tiled=True)
    work = slab.reshape(rows, nx, ng, depth).transpose(2, 0, 1, 3)
    work = lax.all_to_all(work, GROUP, 0, 0, tiled=True).reshape(ng * rows, nx * depth)

    products = lax.psum(matmul(work, basis), ("zl", "y", "prow"))

    scaled = [None] * count
    for k in reversed(range(count)):
        part = products[:, k * width : (k + 1) * width]
        for j in range(k + 1, count):
            block = gram[(j - 1) * width : j * width, k * width : (k + 1) * width]
            part = part - matmul(scaled[j], block)
        scaled[k] = matmul(part, tfactors[k].T)
    scaled = jnp.concatenate(scaled, axis=1)

    work = work - matmul(scaled, basis.T)
    work = work.reshape(ng, rows, nx, depth)
    work = lax.all_to_all(work, GROUP, 0, 0, tiled=True)
    return work.transpose(1, 2, 0, 3).reshape(rows, cols)


def solution(mesh):
    devices = mesh.devices.reshape((mesh.shape["prow"],) + PCOL_PARTS)
    fine = Mesh(devices, ("prow", "x", "zl", "y"))
    cols = ("x", "zl", "y")
    in_specs = (P(cols, "prow"), P(("prow",) + cols, None), P())
    out_specs = P(cols, "prow")
    return jax.shard_map(per_device, mesh=fine, in_specs=in_specs, out_specs=out_specs, check_vma=False)
```

```python
import jax
import jax.numpy as jnp
from jax import lax
from jax.sharding import Mesh
from jax.sharding import PartitionSpec as P

PCOL_PARTS = (4, 2, 4)
GROUP = ("zl", "y")
REDUCE = ("zl", "y", "prow")
REDUCE_SIZE = 64


def matmul(left, right):
    return jnp.dot(left, right, precision=lax.Precision.HIGHEST, preferred_element_type=jnp.float32)


def per_device(slab, vectors, tfactors):
    rows, cols = slab.shape
    depth = vectors.shape[0]
    count = tfactors.shape[0]
    width = tfactors.shape[1]
    nx = PCOL_PARTS[0]
    ng = PCOL_PARTS[1] * PCOL_PARTS[2]

    basis = lax.all_gather(vectors, "x", axis=0, tiled=True)
    work = slab.reshape(rows, nx, ng, depth).transpose(2, 0, 1, 3)
    work = lax.all_to_all(work, GROUP, 0, 0, tiled=True).reshape(ng * rows, nx * depth)

    products = matmul(work, basis)
    gram = matmul(basis[:, width:].T, basis[:, : (count - 1) * width])
    packed = jnp.concatenate([products.reshape(-1), gram.reshape(-1)])
    parts = REDUCE_SIZE
    size = packed.shape[0]
    chunk = -(-size // parts)
    packed = jnp.pad(packed, (0, chunk * parts - size)).reshape(parts, chunk)
    total = jnp.sum(lax.all_to_all(packed, REDUCE, 0, 0, tiled=True), axis=0)
    packed = lax.all_to_all(jnp.broadcast_to(total, (parts, chunk)), REDUCE, 0, 0, tiled=True)
    packed = packed.reshape(-1)[:size]
    products = packed[: products.size].reshape(products.shape)
    gram = packed[products.size :].reshape(gram.shape)

    scaled = [None] * count
    for k in reversed(range(count)):
        part = products[:, k * width : (k + 1) * width]
        for j in range(k + 1, count):
            block = gram[(j - 1) * width : j * width, k * width : (k + 1) * width]
            part = part - matmul(scaled[j], block)
        scaled[k] = matmul(part, tfactors[k].T)
    scaled = jnp.concatenate(scaled, axis=1)

    work = work - matmul(scaled, basis.T)
    work = work.reshape(ng, rows, nx, depth)
    work = lax.all_to_all(work, GROUP, 0, 0, tiled=True)
    return work.transpose(1, 2, 0, 3).reshape(rows, cols)


def solution(mesh):
    devices = mesh.devices.reshape((mesh.shape["prow"],) + PCOL_PARTS)
    fine = Mesh(devices, ("prow", "x", "zl", "y"))
    cols = ("x", "zl", "y")
    in_specs = (P(cols, "prow"), P(("prow",) + cols, None), P())
    out_specs = P(cols, "prow")
    return jax.shard_map(per_device, mesh=fine, in_specs=in_specs, out_specs=out_specs, check_vma=False)
```

```python
import jax
import jax.numpy as jnp
from jax import lax
from jax.sharding import Mesh
from jax.sharding import PartitionSpec as P

PCOL_PARTS = (4, 2, 4)
GROUP = ("x", "zl")
PROW_SIZE = 8


def matmul(left, right):
    return jnp.dot(left, right, precision=lax.Precision.HIGHEST, preferred_element_type=jnp.float32)


def all_reduce(packed, outer, inner, outer_size, inner_size):
    size = packed.shape[0]
    parts = outer_size * inner_size
    chunk = -(-size // parts)
    packed = jnp.pad(packed, (0, chunk * parts - size)).reshape(outer_size, inner_size * chunk)
    total = jnp.sum(lax.all_to_all(packed, outer, 0, 0, tiled=True), axis=0).reshape(inner_size, chunk)
    total = jnp.sum(lax.all_to_all(total, inner, 0, 0, tiled=True), axis=0)
    total = lax.all_to_all(jnp.broadcast_to(total, (inner_size, chunk)), inner, 0, 0, tiled=True)
    total = jnp.broadcast_to(total.reshape(1, inner_size * chunk), (outer_size, inner_size * chunk))
    total = lax.all_to_all(total, outer, 0, 0, tiled=True)
    return total.reshape(-1)[:size]


def per_device(slab, vectors, tfactors):
    rows, cols = slab.shape
    count = tfactors.shape[0]
    width = tfactors.shape[1]
    ng = PCOL_PARTS[0] * PCOL_PARTS[1]
    nprow = PROW_SIZE

    basis = lax.all_gather(vectors, "y", axis=0, tiled=True)
    work = lax.all_to_all(slab, GROUP, 1, 0, tiled=True)

    products = matmul(work, basis)
    gram = matmul(basis[:, width:].T, basis[:, : (count - 1) * width])
    packed = jnp.concatenate([products.reshape(-1), gram.reshape(-1)])
    packed = all_reduce(packed, GROUP, "prow", ng, nprow)
    products = packed[: products.size].reshape(products.shape)
    gram = packed[products.size :].reshape(gram.shape)

    scaled = [None] * count
    for k in reversed(range(count)):
        part = products[:, k * width : (k + 1) * width]
        for j in range(k + 1, count):
            block = gram[(j - 1) * width : j * width, k * width : (k + 1) * width]
            part = part - matmul(scaled[j], block)
        scaled[k] = matmul(part, tfactors[k].T)
    scaled = jnp.concatenate(scaled, axis=1)

    work = work - matmul(scaled, basis.T)
    return lax.all_to_all(work, GROUP, 0, 1, tiled=True)


def solution(mesh):
    devices = mesh.devices.reshape((mesh.shape["prow"],) + PCOL_PARTS)
    fine = Mesh(devices, ("prow", "x", "zl", "y"))
    cols = ("x", "zl", "y")
    in_specs = (P(cols, "prow"), P(("prow",) + cols, None), P())
    out_specs = P(cols, "prow")
    return jax.shard_map(per_device, mesh=fine, in_specs=in_specs, out_specs=out_specs, check_vma=False)
```

```python
import jax
import jax.numpy as jnp
from jax import lax
from jax.sharding import Mesh
from jax.sharding import PartitionSpec as P

PCOL_PARTS = (4, 2, 4)
GROUP = ("x", "zl")
PROW_SIZE = 8


def matmul(left, right):
    return jnp.dot(left, right, precision=lax.Precision.HIGH, preferred_element_type=jnp.float32)


def all_reduce(packed, outer, inner, outer_size, inner_size):
    size = packed.shape[0]
    parts = outer_size * inner_size
    chunk = -(-size // parts)
    packed = jnp.pad(packed, (0, chunk * parts - size)).reshape(outer_size, inner_size * chunk)
    total = jnp.sum(lax.all_to_all(packed, outer, 0, 0, tiled=True), axis=0).reshape(inner_size, chunk)
    total = jnp.sum(lax.all_to_all(total, inner, 0, 0, tiled=True), axis=0)
    total = lax.all_to_all(jnp.broadcast_to(total, (inner_size, chunk)), inner, 0, 0, tiled=True)
    total = jnp.broadcast_to(total.reshape(1, inner_size * chunk), (outer_size, inner_size * chunk))
    total = lax.all_to_all(total, outer, 0, 0, tiled=True)
    return total.reshape(-1)[:size]


def per_device(slab, vectors, tfactors):
    rows, cols = slab.shape
    count = tfactors.shape[0]
    width = tfactors.shape[1]
    ng = PCOL_PARTS[0] * PCOL_PARTS[1]
    nprow = PROW_SIZE

    basis = lax.all_gather(vectors, "y", axis=0, tiled=True)
    work = lax.all_to_all(slab, GROUP, 1, 0, tiled=True)

    products = matmul(work, basis)
    grams = [matmul(basis[:, j * width : (j + 1) * width].T, basis[:, : j * width]) for j in range(1, count)]
    packed = jnp.concatenate([products.reshape(-1)] + [g.reshape(-1) for g in grams])
    packed = all_reduce(packed, GROUP, "prow", ng, nprow)
    products, offset = packed[: products.size].reshape(products.shape), products.size
    for j in range(1, count):
        size = grams[j - 1].size
        grams[j - 1], offset = packed[offset : offset + size].reshape(grams[j - 1].shape), offset + size

    scaled = [None] * count
    for k in reversed(range(count)):
        part = products[:, k * width : (k + 1) * width]
        for j in range(k + 1, count):
            block = grams[j - 1][:, k * width : (k + 1) * width]
            part = part - matmul(scaled[j], block)
        scaled[k] = matmul(part, tfactors[k].T)
    scaled = jnp.concatenate(scaled, axis=1)

    work = work - matmul(scaled, basis.T)
    return lax.all_to_all(work, GROUP, 0, 1, tiled=True)


def solution(mesh):
    devices = mesh.devices.reshape((mesh.shape["prow"],) + PCOL_PARTS)
    fine = Mesh(devices, ("prow", "x", "zl", "y"))
    cols = ("x", "zl", "y")
    in_specs = (P(cols, "prow"), P(("prow",) + cols, None), P())
    out_specs = P(cols, "prow")
    return jax.shard_map(per_device, mesh=fine, in_specs=in_specs, out_specs=out_specs, check_vma=False)
```

```python
import jax
import jax.numpy as jnp
from jax import lax
from jax.sharding import Mesh
from jax.sharding import PartitionSpec as P

PCOL_PARTS = (4, 2, 4)
GROUP = ("x", "zl")
PROW_SIZE = 8


def matmul(left, right):
    return jnp.dot(left, right, precision=lax.Precision.HIGH, preferred_element_type=jnp.float32)


def all_reduce(packed, outer, inner, outer_size, inner_size):
    size = packed.shape[0]
    chunk = -(-size // outer_size)
    packed = jnp.pad(packed, (0, chunk * outer_size - size)).reshape(outer_size, chunk)
    total = jnp.sum(lax.all_to_all(packed, outer, 0, 0, tiled=True), axis=0)
    bit = 1
    while bit < inner_size:
        total = total + lax.ppermute(total, inner, [(i, i ^ bit) for i in range(inner_size)])
        bit *= 2
    total = lax.all_to_all(jnp.broadcast_to(total, (outer_size, chunk)), outer, 0, 0, tiled=True)
    return total.reshape(-1)[:size]


def per_device(slab, vectors, tfactors):
    rows, cols = slab.shape
    count = tfactors.shape[0]
    width = tfactors.shape[1]
    ng = PCOL_PARTS[0] * PCOL_PARTS[1]
    nprow = PROW_SIZE

    basis = lax.all_gather(vectors, "y", axis=0, tiled=True)
    work = lax.all_to_all(slab, GROUP, 1, 0, tiled=True)

    products = matmul(work, basis)
    grams = [matmul(basis[:, j * width : (j + 1) * width].T, basis[:, : j * width]) for j in range(1, count)]
    packed = jnp.concatenate([products.reshape(-1)] + [g.reshape(-1) for g in grams])
    packed = all_reduce(packed, GROUP, "prow", ng, nprow)
    products, offset = packed[: products.size].reshape(products.shape), products.size
    for j in range(1, count):
        size = grams[j - 1].size
        grams[j - 1], offset = packed[offset : offset + size].reshape(grams[j - 1].shape), offset + size

    scaled = [None] * count
    for k in reversed(range(count)):
        part = products[:, k * width : (k + 1) * width]
        for j in range(k + 1, count):
            block = grams[j - 1][:, k * width : (k + 1) * width]
            part = part - matmul(scaled[j], block)
        scaled[k] = matmul(part, tfactors[k].T)
    scaled = jnp.concatenate(scaled, axis=1)

    work = work - matmul(scaled, basis.T)
    return lax.all_to_all(work, GROUP, 0, 1, tiled=True)


def solution(mesh):
    devices = mesh.devices.reshape((mesh.shape["prow"],) + PCOL_PARTS)
    fine = Mesh(devices, ("prow", "x", "zl", "y"))
    cols = ("x", "zl", "y")
    in_specs = (P(cols, "prow"), P(("prow",) + cols, None), P())
    out_specs = P(cols, "prow")
    return jax.shard_map(per_device, mesh=fine, in_specs=in_specs, out_specs=out_specs, check_vma=False)
```

```python
import jax
import jax.numpy as jnp
from jax import lax
from jax.sharding import Mesh
from jax.sharding import PartitionSpec as P

PCOL_PARTS = (4, 2, 4)
GROUP = ("x", "zl")
PROW_SIZE = 8


def matmul(left, right):
    return jnp.dot(left, right, precision=lax.Precision.HIGH, preferred_element_type=jnp.float32)


def all_reduce(packed, outer, inner, outer_size, inner_size):
    size = packed.shape[0]
    chunk = -(-size // outer_size)
    packed = jnp.pad(packed, (0, chunk * outer_size - size)).reshape(outer_size, chunk)
    total = jnp.sum(lax.all_to_all(packed, outer, 0, 0, tiled=True), axis=0)
    bit = 1
    while bit < inner_size:
        total = total + lax.ppermute(total, inner, [(i, i ^ bit) for i in range(inner_size)])
        bit *= 2
    total = lax.all_to_all(jnp.broadcast_to(total, (outer_size, chunk)), outer, 0, 0, tiled=True)
    return total.reshape(-1)[:size]


def gather_ring(block, axis, size):
    right = [(i, (i + 1) % size) for i in range(size)]
    left = [(i, (i - 1) % size) for i in range(size)]
    from_left = lax.ppermute(block, axis, right)
    from_right = lax.ppermute(block, axis, left)
    half = block.shape[0] // 2
    far_first = lax.ppermute(from_left[:half], axis, right)
    far_second = lax.ppermute(from_right[half:], axis, left)
    ordered = jnp.concatenate([block, from_right, far_first, far_second, from_left], axis=0)
    shift = lax.axis_index(axis) * block.shape[0]
    ordered = jnp.concatenate([ordered, ordered], axis=0)
    return lax.dynamic_slice_in_dim(ordered, (size * block.shape[0] - shift) % (size * block.shape[0]), size * block.shape[0], axis=0)


def per_device(slab, vectors, tfactors):
    rows, cols = slab.shape
    count = tfactors.shape[0]
    width = tfactors.shape[1]
    ng = PCOL_PARTS[0] * PCOL_PARTS[1]
    nprow = PROW_SIZE

    basis = gather_ring(vectors, "y", PCOL_PARTS[2])
    work = lax.all_to_all(slab, GROUP, 1, 0, tiled=True)

    products = matmul(work, basis)
    grams = [matmul(basis[:, j * width : (j + 1) * width].T, basis[:, : j * width]) for j in range(1, count)]
    packed = jnp.concatenate([products.reshape(-1)] + [g.reshape(-1) for g in grams])
    packed = all_reduce(packed, GROUP, "prow", ng, nprow)
    products, offset = packed[: products.size].reshape(products.shape), products.size
    for j in range(1, count):
        size = grams[j - 1].size
        grams[j - 1], offset = packed[offset : offset + size].reshape(grams[j - 1].shape), offset + size

    scaled = [None] * count
    for k in reversed(range(count)):
        part = products[:, k * width : (k + 1) * width]
        for j in range(k + 1, count):
            block = grams[j - 1][:, k * width : (k + 1) * width]
            part = part - matmul(scaled[j], block)
        scaled[k] = matmul(part, tfactors[k].T)
    scaled = jnp.concatenate(scaled, axis=1)

    work = work - matmul(scaled, basis.T)
    return lax.all_to_all(work, GROUP, 0, 1, tiled=True)


def solution(mesh):
    devices = mesh.devices.reshape((mesh.shape["prow"],) + PCOL_PARTS)
    fine = Mesh(devices, ("prow", "x", "zl", "y"))
    cols = ("x", "zl", "y")
    in_specs = (P(cols, "prow"), P(("prow",) + cols, None), P())
    out_specs = P(cols, "prow")
    return jax.shard_map(per_device, mesh=fine, in_specs=in_specs, out_specs=out_specs, check_vma=False)
```

```python
import jax
import jax.numpy as jnp
from jax import lax
from jax.sharding import Mesh
from jax.sharding import PartitionSpec as P

PCOL_PARTS = (4, 2, 4)
GROUP = ("x", "zl")
PROW_SIZE = 8


def matmul(left, right):
    return jnp.dot(left, right, precision=lax.Precision.HIGH, preferred_element_type=jnp.float32)


def all_reduce(packed, outer, inner, outer_size, inner_size):
    rows, lanes = packed.shape
    chunk = -(-rows // (8 * outer_size)) * 8
    packed = jnp.pad(packed, ((0, chunk * outer_size - rows), (0, 0))).reshape(outer_size, chunk, lanes)
    total = jnp.sum(lax.all_to_all(packed, outer, 0, 0, tiled=True), axis=0)
    bit = 1
    while bit < inner_size:
        total = total + lax.ppermute(total, inner, [(i, i ^ bit) for i in range(inner_size)])
        bit *= 2
    total = lax.all_to_all(jnp.broadcast_to(total, (outer_size, chunk, lanes)), outer, 0, 0, tiled=True)
    return total.reshape(outer_size * chunk, lanes)[:rows]


def gather_ring(block, axis, size):
    right = [(i, (i + 1) % size) for i in range(size)]
    left = [(i, (i - 1) % size) for i in range(size)]
    from_left = lax.ppermute(block, axis, right)
    from_right = lax.ppermute(block, axis, left)
    half = block.shape[0] // 2
    far_first = lax.ppermute(from_left[:half], axis, right)
    far_second = lax.ppermute(from_right[half:], axis, left)
    ordered = jnp.concatenate([block, from_right, far_first, far_second, from_left], axis=0)
    shift = lax.axis_index(axis) * block.shape[0]
    ordered = jnp.concatenate([ordered, ordered], axis=0)
    return lax.dynamic_slice_in_dim(ordered, (size * block.shape[0] - shift) % (size * block.shape[0]), size * block.shape[0], axis=0)


def per_device(slab, vectors, tfactors):
    rows, cols = slab.shape
    count = tfactors.shape[0]
    width = tfactors.shape[1]
    ng = PCOL_PARTS[0] * PCOL_PARTS[1]
    nprow = PROW_SIZE

    basis = gather_ring(vectors, "y", PCOL_PARTS[2])
    work = lax.all_to_all(slab, GROUP, 1, 0, tiled=True)

    blocks = [basis[:, k * width : (k + 1) * width] for k in range(count)]
    products = [matmul(work, blocks[k]) for k in range(count)]
    grams = [matmul(blocks[j].T, basis[:, : j * width]) for j in range(1, count)]
    grams = [g[:, k * width : (k + 1) * width] for j, g in enumerate(grams, 1) for k in range(j)]
    packed = all_reduce(jnp.concatenate(products + grams, axis=0), GROUP, "prow", ng, nprow)
    span = products[0].shape[0]
    products = [packed[k * span : (k + 1) * span] for k in range(count)]
    offset = count * span
    gram = {}
    for j in range(1, count):
        for k in range(j):
            gram[j, k], offset = packed[offset : offset + width], offset + width

    scaled = [None] * count
    for k in reversed(range(count)):
        part = products[k]
        for j in range(k + 1, count):
            part = part - matmul(scaled[j], gram[j, k])
        scaled[k] = matmul(part, tfactors[k].T)
    scaled = jnp.concatenate(scaled, axis=1)

    work = work - matmul(scaled, basis.T)
    return lax.all_to_all(work, GROUP, 0, 1, tiled=True)


def solution(mesh):
    devices = mesh.devices.reshape((mesh.shape["prow"],) + PCOL_PARTS)
    fine = Mesh(devices, ("prow", "x", "zl", "y"))
    cols = ("x", "zl", "y")
    in_specs = (P(cols, "prow"), P(("prow",) + cols, None), P())
    out_specs = P(cols, "prow")
    return jax.shard_map(per_device, mesh=fine, in_specs=in_specs, out_specs=out_specs, check_vma=False)
```

```python
import jax
import jax.numpy as jnp
from jax import lax
from jax.sharding import Mesh
from jax.sharding import PartitionSpec as P

PCOL_PARTS = (4, 2, 4)
GROUP = ("x", "zl")
PROW_SIZE = 8


def matmul(left, right):
    return jnp.dot(left, right, precision=lax.Precision.HIGH, preferred_element_type=jnp.float32)


def all_reduce(packed, outer, inner, outer_size, inner_size):
    rows, lanes = packed.shape
    chunk = -(-rows // (8 * outer_size)) * 8
    packed = jnp.pad(packed, ((0, chunk * outer_size - rows), (0, 0))).reshape(outer_size, chunk, lanes)
    total = jnp.sum(lax.all_to_all(packed, outer, 0, 0, tiled=True), axis=0)
    bit = 1
    while bit < inner_size:
        total = total + lax.ppermute(total, inner, [(i, i ^ bit) for i in range(inner_size)])
        bit *= 2
    total = lax.all_to_all(jnp.broadcast_to(total, (outer_size, chunk, lanes)), outer, 0, 0, tiled=True)
    return total.reshape(outer_size * chunk, lanes)[:rows]


def gather_ring(block, axis, size):
    right = [(i, (i + 1) % size) for i in range(size)]
    left = [(i, (i - 1) % size) for i in range(size)]
    from_left = lax.ppermute(block, axis, right)
    from_right = lax.ppermute(block, axis, left)
    half = block.shape[0] // 2
    far_first = lax.ppermute(from_left[:half], axis, right)
    far_second = lax.ppermute(from_right[half:], axis, left)
    ordered = jnp.concatenate([block, from_right, far_first, far_second, from_left], axis=0)
    shift = lax.axis_index(axis) * block.shape[0]
    ordered = jnp.concatenate([ordered, ordered], axis=0)
    return lax.dynamic_slice_in_dim(ordered, (size * block.shape[0] - shift) % (size * block.shape[0]), size * block.shape[0], axis=0)


def per_device(slab, vectors, tfactors):
    rows, cols = slab.shape
    count = tfactors.shape[0]
    width = tfactors.shape[1]
    ng = PCOL_PARTS[0] * PCOL_PARTS[1]
    nprow = PROW_SIZE

    basis = gather_ring(vectors, "y", PCOL_PARTS[2])
    work = lax.all_to_all(slab, GROUP, 1, 0, tiled=True)

    products = matmul(work, basis)
    grams = jnp.concatenate([matmul(basis[:, j * width : (j + 1) * width].T, basis[:, : j * width]) for j in range(1, count)], axis=1)
    lanes = products.shape[1]
    packed = jnp.concatenate([products, grams.reshape(-1, lanes)], axis=0)
    half = lanes // 2
    packed = jnp.concatenate([all_reduce(packed[:, :half], GROUP, "prow", ng, nprow), all_reduce(packed[:, half:], GROUP, "prow", ng, nprow)], axis=1)
    span = products.shape[0]
    products = [packed[:span, k * width : (k + 1) * width] for k in range(count)]
    grams = packed[span:].reshape(grams.shape)
    gram, offset = {}, 0
    for j in range(1, count):
        for k in range(j):
            gram[j, k], offset = grams[:, offset : offset + width], offset + width

    scaled = [None] * count
    for k in reversed(range(count)):
        part = products[k]
        for j in range(k + 1, count):
            part = part - matmul(scaled[j], gram[j, k])
        scaled[k] = matmul(part, tfactors[k].T)
    scaled = jnp.concatenate(scaled, axis=1)

    work = work - matmul(scaled, basis.T)
    return lax.all_to_all(work, GROUP, 0, 1, tiled=True)


def solution(mesh):
    devices = mesh.devices.reshape((mesh.shape["prow"],) + PCOL_PARTS)
    fine = Mesh(devices, ("prow", "x", "zl", "y"))
    cols = ("x", "zl", "y")
    in_specs = (P(cols, "prow"), P(("prow",) + cols, None), P())
    out_specs = P(cols, "prow")
    return jax.shard_map(per_device, mesh=fine, in_specs=in_specs, out_specs=out_specs, check_vma=False)
```

```python
import jax
import jax.numpy as jnp
from jax import lax
from jax.sharding import Mesh
from jax.sharding import PartitionSpec as P

PCOL_PARTS = (4, 2, 4)
GROUP = ("x", "zl")
PROW_SIZE = 8


def matmul(left, right):
    return jnp.dot(left, right, precision=lax.Precision.HIGH, preferred_element_type=jnp.float32)


def all_reduce(packed, outer, inner, outer_size, inner_size):
    rows, lanes = packed.shape
    chunk = -(-rows // (8 * outer_size)) * 8
    packed = jnp.pad(packed, ((0, chunk * outer_size - rows), (0, 0))).reshape(outer_size, chunk, lanes)
    total = jnp.sum(lax.all_to_all(packed, outer, 0, 0, tiled=True), axis=0)
    bit = 1
    while bit < inner_size:
        total = total + lax.ppermute(total, inner, [(i, i ^ bit) for i in range(inner_size)])
        bit *= 2
    total = lax.all_to_all(jnp.broadcast_to(total, (outer_size, chunk, lanes)), outer, 0, 0, tiled=True)
    return total.reshape(outer_size * chunk, lanes)[:rows]


def gather_ring(block, axis, size):
    right = [(i, (i + 1) % size) for i in range(size)]
    left = [(i, (i - 1) % size) for i in range(size)]
    from_left = lax.ppermute(block, axis, right)
    from_right = lax.ppermute(block, axis, left)
    half = block.shape[0] // 2
    far_first = lax.ppermute(from_left[:half], axis, right)
    far_second = lax.ppermute(from_right[half:], axis, left)
    ordered = jnp.concatenate([block, from_right, far_first, far_second, from_left], axis=0)
    shift = lax.axis_index(axis) * block.shape[0]
    ordered = jnp.concatenate([ordered, ordered], axis=0)
    return lax.dynamic_slice_in_dim(ordered, (size * block.shape[0] - shift) % (size * block.shape[0]), size * block.shape[0], axis=0)


def per_device(slab, vectors, tfactors):
    rows, cols = slab.shape
    count = tfactors.shape[0]
    width = tfactors.shape[1]
    ng = PCOL_PARTS[0] * PCOL_PARTS[1]
    nprow = PROW_SIZE

    basis = gather_ring(vectors, "y", PCOL_PARTS[2])
    work = lax.all_to_all(slab, GROUP, 1, 0, tiled=True)

    products = matmul(work, basis)
    grams = jnp.concatenate([matmul(basis[:, j * width : (j + 1) * width].T, basis[:, : j * width]) for j in range(1, count)], axis=1)
    lanes = products.shape[1]
    packed = jnp.concatenate([products, grams.reshape(-1, lanes)], axis=0)
    packed = all_reduce(packed, GROUP, "prow", ng, nprow)
    span = products.shape[0]
    products = [packed[:span, k * width : (k + 1) * width] for k in range(count)]
    grams = packed[span:].reshape(grams.shape)
    gram, offset = {}, 0
    for j in range(1, count):
        for k in range(j):
            gram[j, k], offset = grams[:, offset : offset + width], offset + width

    scaled = [None] * count
    for k in reversed(range(count)):
        part = products[k]
        for j in range(k + 1, count):
            part = part - matmul(scaled[j], gram[j, k])
        scaled[k] = matmul(part, tfactors[k].T)
    scaled = jnp.concatenate(scaled, axis=1)

    work = work - matmul(scaled, basis.T)
    return lax.all_to_all(work, GROUP, 0, 1, tiled=True)


def solution(mesh):
    devices = mesh.devices.reshape((mesh.shape["prow"],) + PCOL_PARTS)
    fine = Mesh(devices, ("prow", "x", "zl", "y"))
    cols = ("x", "zl", "y")
    in_specs = (P(cols, "prow"), P(("prow",) + cols, None), P())
    out_specs = P(cols, "prow")
    return jax.shard_map(per_device, mesh=fine, in_specs=in_specs, out_specs=out_specs, check_vma=False)
```

```python
import jax
import jax.numpy as jnp
from jax import lax
from jax.sharding import Mesh
from jax.sharding import PartitionSpec as P

PCOL_PARTS = (4, 2, 4)
GROUP = ("x", "zl")
PROW_SIZE = 8


def matmul(left, right):
    return jnp.dot(left, right, precision=lax.Precision.HIGH, preferred_element_type=jnp.float32)


def all_reduce(packed, outer, inner, outer_size, inner_size):
    rows, lanes = packed.shape
    chunk = -(-rows // (8 * outer_size)) * 8
    packed = jnp.pad(packed, ((0, chunk * outer_size - rows), (0, 0))).reshape(outer_size, chunk, lanes)
    total = jnp.sum(lax.all_to_all(packed, outer, 0, 0, tiled=True), axis=0)
    bit = 1
    while bit < inner_size:
        total = total + lax.ppermute(total, inner, [(i, i ^ bit) for i in range(inner_size)])
        bit *= 2
    total = lax.all_to_all(jnp.broadcast_to(total, (outer_size, chunk, lanes)), outer, 0, 0, tiled=True)
    return total.reshape(outer_size * chunk, lanes)[:rows]


def gather_ring(block, axis, size):
    right = [(i, (i + 1) % size) for i in range(size)]
    left = [(i, (i - 1) % size) for i in range(size)]
    from_left = lax.ppermute(block, axis, right)
    from_right = lax.ppermute(block, axis, left)
    half = block.shape[0] // 2
    far_first = lax.ppermute(from_left[:half], axis, right)
    far_second = lax.ppermute(from_right[half:], axis, left)
    ordered = jnp.concatenate([block, from_right, far_first, far_second, from_left], axis=0)
    shift = lax.axis_index(axis) * block.shape[0]
    ordered = jnp.concatenate([ordered, ordered], axis=0)
    return lax.dynamic_slice_in_dim(ordered, (size * block.shape[0] - shift) % (size * block.shape[0]), size * block.shape[0], axis=0)


def per_device(slab, vectors, tfactors):
    rows, cols = slab.shape
    count = tfactors.shape[0]
    width = tfactors.shape[1]
    ng = PCOL_PARTS[0] * PCOL_PARTS[1]
    nprow = PROW_SIZE

    basis = gather_ring(vectors, "y", PCOL_PARTS[2])
    work = lax.all_to_all(slab, GROUP, 1, 0, tiled=True)

    products = matmul(work, basis)
    grams = jnp.concatenate([matmul(basis[:, j * width : (j + 1) * width].T, basis[:, : j * width]) for j in range(1, count)], axis=1)
    lanes = products.shape[1]
    packed = jnp.concatenate([products, grams.reshape(-1, lanes)], axis=0)
    packed = all_reduce(packed, GROUP, "prow", ng, nprow)
    span = products.shape[0]
    products = [packed[:span, k * width : (k + 1) * width] for k in range(count)]
    grams = packed[span:].reshape(grams.shape)
    gram, offset = {}, 0
    for j in range(1, count):
        for k in range(j):
            gram[j, k], offset = grams[:, offset : offset + width], offset + width

    scaled = [None] * count
    for k in reversed(range(count)):
        part = products[k]
        for j in range(k + 1, count):
            part = part - matmul(scaled[j], gram[j, k])
        scaled[k] = matmul(part, tfactors[k].T)
    scaled = jnp.concatenate(scaled, axis=1)

    work = work.reshape(ng, rows, -1)
    scaled = scaled.reshape(ng, rows, -1)
    half = rows // 2
    outs = []
    for part in (slice(0, half), slice(half, rows)):
        piece = work[:, part] - matmul(scaled[:, part].reshape(ng * half, -1), basis.T).reshape(ng, half, -1)
        outs.append(lax.all_to_all(piece, GROUP, 0, 2, tiled=True).reshape(half, cols))
    return jnp.concatenate(outs, axis=0)


def solution(mesh):
    devices = mesh.devices.reshape((mesh.shape["prow"],) + PCOL_PARTS)
    fine = Mesh(devices, ("prow", "x", "zl", "y"))
    cols = ("x", "zl", "y")
    in_specs = (P(cols, "prow"), P(("prow",) + cols, None), P())
    out_specs = P(cols, "prow")
    return jax.shard_map(per_device, mesh=fine, in_specs=in_specs, out_specs=out_specs, check_vma=False)
```

```python
import jax
import jax.numpy as jnp
from jax import lax
from jax.sharding import Mesh
from jax.sharding import PartitionSpec as P

PCOL_PARTS = (4, 2, 4)
GROUP = ("x", "zl")
PROW_SIZE = 8


def matmul(left, right):
    return jnp.dot(left, right, precision=lax.Precision.HIGH, preferred_element_type=jnp.float32)


def all_reduce(packed, outer, inner, outer_size, inner_size):
    rows, lanes = packed.shape
    chunk = -(-rows // (8 * outer_size)) * 8
    packed = jnp.pad(packed, ((0, chunk * outer_size - rows), (0, 0))).reshape(outer_size, chunk, lanes)
    total = jnp.sum(lax.all_to_all(packed, outer, 0, 0, tiled=True), axis=0)
    bit = 1
    while bit < inner_size:
        total = total + lax.ppermute(total, inner, [(i, i ^ bit) for i in range(inner_size)])
        bit *= 2
    total = lax.all_to_all(jnp.broadcast_to(total, (outer_size, chunk, lanes)), outer, 0, 0, tiled=True)
    return total.reshape(outer_size * chunk, lanes)[:rows]


def gather_ring(block, axis, size):
    right = [(i, (i + 1) % size) for i in range(size)]
    left = [(i, (i - 1) % size) for i in range(size)]
    from_left = lax.ppermute(block, axis, right)
    from_right = lax.ppermute(block, axis, left)
    half = block.shape[0] // 2
    far_first = lax.ppermute(from_left[:half], axis, right)
    far_second = lax.ppermute(from_right[half:], axis, left)
    ordered = jnp.concatenate([block, from_right, far_first, far_second, from_left], axis=0)
    shift = lax.axis_index(axis) * block.shape[0]
    ordered = jnp.concatenate([ordered, ordered], axis=0)
    return lax.dynamic_slice_in_dim(ordered, (size * block.shape[0] - shift) % (size * block.shape[0]), size * block.shape[0], axis=0)


def per_device(slab, vectors, tfactors):
    rows, cols = slab.shape
    count = tfactors.shape[0]
    width = tfactors.shape[1]
    ng = PCOL_PARTS[0] * PCOL_PARTS[1]
    nprow = PROW_SIZE

    basis = gather_ring(vectors, "y", PCOL_PARTS[2])
    work = lax.all_to_all(slab, GROUP, 1, 0, tiled=True)

    products = matmul(work, basis)
    grams = jnp.concatenate([matmul(basis[:, j * width : (j + 1) * width].T, basis[:, : j * width]) for j in range(1, count)], axis=1)
    lanes = products.shape[1]
    packed = jnp.concatenate([products, grams.reshape(-1, lanes)], axis=0)
    packed = all_reduce(packed, GROUP, "prow", ng, nprow)
    span = products.shape[0]
    grams = packed[span:].reshape(grams.shape)
    gram, offset = {}, 0
    for j in range(1, count):
        for k in range(j):
            gram[j, k], offset = grams[:, offset : offset + width], offset + width

    diagonal = jnp.zeros((count * width, count * width), tfactors.dtype)
    for k in range(count):
        diagonal = diagonal.at[k * width : (k + 1) * width, k * width : (k + 1) * width].set(tfactors[k].T)
    products = matmul(packed[:span], diagonal)
    scaled = [None] * count
    for k in reversed(range(count)):
        part = products[:, k * width : (k + 1) * width]
        if k + 1 < count:
            later = list(range(count - 1, k, -1))
            weights = matmul(jnp.concatenate([gram[j, k] for j in later], axis=0), tfactors[k].T)
            part = part - matmul(jnp.concatenate([scaled[j] for j in later], axis=1), weights)
        scaled[k] = part
    scaled = jnp.concatenate(scaled, axis=1)

    work = work - matmul(scaled, basis.T)
    return lax.all_to_all(work, GROUP, 0, 1, tiled=True)


def solution(mesh):
    devices = mesh.devices.reshape((mesh.shape["prow"],) + PCOL_PARTS)
    fine = Mesh(devices, ("prow", "x", "zl", "y"))
    cols = ("x", "zl", "y")
    in_specs = (P(cols, "prow"), P(("prow",) + cols, None), P())
    out_specs = P(cols, "prow")
    return jax.shard_map(per_device, mesh=fine, in_specs=in_specs, out_specs=out_specs, check_vma=False)
```

```python
import jax
import jax.numpy as jnp
from jax import lax
from jax.sharding import Mesh
from jax.sharding import PartitionSpec as P

PCOL_PARTS = (4, 2, 4)
GROUP = ("x", "zl")
PROW_SIZE = 8


def matmul(left, right):
    return jnp.dot(left, right, precision=lax.Precision.HIGH, preferred_element_type=jnp.float32)


def all_reduce(packed, outer, inner, outer_size, inner_size):
    rows, lanes = packed.shape
    chunk = -(-rows // (8 * outer_size)) * 8
    packed = jnp.pad(packed, ((0, chunk * outer_size - rows), (0, 0))).reshape(outer_size, chunk, lanes)
    total = jnp.sum(lax.all_to_all(packed, outer, 0, 0, tiled=True), axis=0)
    bit = 1
    while bit < inner_size:
        total = total + lax.ppermute(total, inner, [(i, i ^ bit) for i in range(inner_size)])
        bit *= 2
    total = lax.all_to_all(jnp.broadcast_to(total, (outer_size, chunk, lanes)), outer, 0, 0, tiled=True)
    return total.reshape(outer_size * chunk, lanes)[:rows]


def gather_ring(block, axis, size):
    right = [(i, (i + 1) % size) for i in range(size)]
    left = [(i, (i - 1) % size) for i in range(size)]
    from_left = lax.ppermute(block, axis, right)
    from_right = lax.ppermute(block, axis, left)
    half = block.shape[0] // 2
    far_first = lax.ppermute(from_left[:half], axis, right)
    far_second = lax.ppermute(from_right[half:], axis, left)
    return jnp.concatenate([block, from_right, far_first, far_second, from_left], axis=0)


def rotate(chunks, shift, size):
    width = chunks.shape[-1]
    doubled = jnp.concatenate([chunks, chunks], axis=-1)
    start = ((size - shift) % size) * (width // size)
    return lax.dynamic_slice_in_dim(doubled, start, width, axis=chunks.ndim - 1)


def per_device(slab, vectors, tfactors):
    rows, cols = slab.shape
    count = tfactors.shape[0]
    width = tfactors.shape[1]
    ng = PCOL_PARTS[0] * PCOL_PARTS[1]
    nprow = PROW_SIZE

    ny = PCOL_PARTS[2]
    depth = vectors.shape[0]
    turn = lax.axis_index("y")
    basis = gather_ring(vectors, "y", ny)
    work = rotate(slab.reshape(rows, ng, ny * depth), -turn, ny).reshape(rows, cols)
    work = lax.all_to_all(work, GROUP, 1, 0, tiled=True)

    products = matmul(work, basis)
    grams = jnp.concatenate([matmul(basis[:, j * width : (j + 1) * width].T, basis[:, : j * width]) for j in range(1, count)], axis=1)
    lanes = products.shape[1]
    packed = jnp.concatenate([products, grams.reshape(-1, lanes)], axis=0)
    packed = all_reduce(packed, GROUP, "prow", ng, nprow)
    span = products.shape[0]
    products = [packed[:span, k * width : (k + 1) * width] for k in range(count)]
    grams = packed[span:].reshape(grams.shape)
    gram, offset = {}, 0
    for j in range(1, count):
        for k in range(j):
            gram[j, k], offset = grams[:, offset : offset + width], offset + width

    scaled = [None] * count
    for k in reversed(range(count)):
        part = products[k]
        for j in range(k + 1, count):
            part = part - matmul(scaled[j], gram[j, k])
        scaled[k] = matmul(part, tfactors[k].T)
    scaled = jnp.concatenate(scaled, axis=1)

    work = work - matmul(scaled, basis.T)
    work = lax.all_to_all(work, GROUP, 0, 1, tiled=True)
    return rotate(work.reshape(rows, ng, ny * depth), turn, ny).reshape(rows, cols)


def solution(mesh):
    devices = mesh.devices.reshape((mesh.shape["prow"],) + PCOL_PARTS)
    fine = Mesh(devices, ("prow", "x", "zl", "y"))
    cols = ("x", "zl", "y")
    in_specs = (P(cols, "prow"), P(("prow",) + cols, None), P())
    out_specs = P(cols, "prow")
    return jax.shard_map(per_device, mesh=fine, in_specs=in_specs, out_specs=out_specs, check_vma=False)
```

```python
import jax
import jax.numpy as jnp
from jax import lax
from jax.sharding import Mesh
from jax.sharding import PartitionSpec as P

PCOL_PARTS = (4, 2, 4)
GROUP = ("x", "zl")
PROW_SIZE = 8


def matmul(left, right):
    return jnp.dot(left, right, precision=lax.Precision.HIGH, preferred_element_type=jnp.float32)


def all_reduce(packed, outer, inner, outer_size, inner_size):
    rows, lanes = packed.shape
    chunk = -(-rows // (8 * outer_size)) * 8
    packed = jnp.pad(packed, ((0, chunk * outer_size - rows), (0, 0))).reshape(outer_size, chunk, lanes)
    total = jnp.sum(lax.all_to_all(packed, outer, 0, 0, tiled=True), axis=0)
    pairs = [(i, i ^ 1) for i in range(inner_size)]
    first = lax.rem(lax.axis_index(inner), 2) == 0
    half = lanes // 2
    keep = jnp.where(first, total[:, :half], total[:, half:])
    send = jnp.where(first, total[:, half:], total[:, :half])
    mine = keep + lax.ppermute(send, inner, pairs)
    bit = 2
    while bit < inner_size:
        mine = mine + lax.ppermute(mine, inner, [(i, i ^ bit) for i in range(inner_size)])
        bit *= 2
    other = lax.ppermute(mine, inner, pairs)
    total = jnp.where(first, jnp.concatenate([mine, other], axis=1), jnp.concatenate([other, mine], axis=1))
    total = lax.all_to_all(jnp.broadcast_to(total, (outer_size, chunk, lanes)), outer, 0, 0, tiled=True)
    return total.reshape(outer_size * chunk, lanes)[:rows]


def gather_ring(block, axis, size):
    right = [(i, (i + 1) % size) for i in range(size)]
    left = [(i, (i - 1) % size) for i in range(size)]
    from_left = lax.ppermute(block, axis, right)
    from_right = lax.ppermute(block, axis, left)
    half = block.shape[0] // 2
    far_first = lax.ppermute(from_left[:half], axis, right)
    far_second = lax.ppermute(from_right[half:], axis, left)
    return jnp.concatenate([block, from_right, far_first, far_second, from_left], axis=0)


def rotate(chunks, shift, size):
    width = chunks.shape[-1]
    doubled = jnp.concatenate([chunks, chunks], axis=-1)
    start = ((size - shift) % size) * (width // size)
    return lax.dynamic_slice_in_dim(doubled, start, width, axis=chunks.ndim - 1)


def per_device(slab, vectors, tfactors):
    rows, cols = slab.shape
    count = tfactors.shape[0]
    width = tfactors.shape[1]
    ng = PCOL_PARTS[0] * PCOL_PARTS[1]
    nprow = PROW_SIZE

    ny = PCOL_PARTS[2]
    depth = vectors.shape[0]
    turn = lax.axis_index("y")
    basis = gather_ring(vectors, "y", ny)
    work = rotate(slab.reshape(rows, ng, ny * depth), -turn, ny).reshape(rows, cols)
    work = lax.all_to_all(work, GROUP, 1, 0, tiled=True)

    products = matmul(work, basis)
    grams = jnp.concatenate([matmul(basis[:, j * width : (j + 1) * width].T, basis[:, : j * width]) for j in range(1, count)], axis=1)
    lanes = products.shape[1]
    packed = jnp.concatenate([products, grams.reshape(-1, lanes)], axis=0)
    packed = all_reduce(packed, GROUP, "prow", ng, nprow)
    span = products.shape[0]
    grams = packed[span:].reshape(grams.shape)
    gram, offset = {}, 0
    for j in range(1, count):
        for k in range(j):
            gram[j, k], offset = grams[:, offset : offset + width], offset + width

    diagonal = jnp.zeros((count * width, count * width), tfactors.dtype)
    for k in range(count):
        diagonal = diagonal.at[k * width : (k + 1) * width, k * width : (k + 1) * width].set(tfactors[k].T)
    products = matmul(packed[:span], diagonal)
    scaled = [None] * count
    for k in reversed(range(count)):
        part = products[:, k * width : (k + 1) * width]
        if k + 1 < count:
            later = list(range(count - 1, k, -1))
            weights = matmul(jnp.concatenate([gram[j, k] for j in later], axis=0), tfactors[k].T)
            part = part - matmul(jnp.concatenate([scaled[j] for j in later], axis=1), weights)
        scaled[k] = part
    scaled = jnp.concatenate(scaled, axis=1)

    work = work - matmul(scaled, basis.T)
    work = lax.all_to_all(work, GROUP, 0, 1, tiled=True)
    return rotate(work.reshape(rows, ng, ny * depth), turn, ny).reshape(rows, cols)


def solution(mesh):
    devices = mesh.devices.reshape((mesh.shape["prow"],) + PCOL_PARTS)
    fine = Mesh(devices, ("prow", "x", "zl", "y"))
    cols = ("x", "zl", "y")
    in_specs = (P(cols, "prow"), P(("prow",) + cols, None), P())
    out_specs = P(cols, "prow")
    return jax.shard_map(per_device, mesh=fine, in_specs=in_specs, out_specs=out_specs, check_vma=False)
```

```python
import jax
import jax.numpy as jnp
from jax import lax
from jax.sharding import Mesh
from jax.sharding import PartitionSpec as P

PCOL_PARTS = (4, 2, 4)
GROUP = ("x", "zl")
PROW_SIZE = 8


def matmul(left, right):
    return jnp.dot(left, right, precision=lax.Precision.HIGH, preferred_element_type=jnp.float32)


def all_reduce(packed, outer, inner, outer_size, inner_size):
    rows, lanes = packed.shape
    pairs = [(i, i ^ 1) for i in range(inner_size)]
    first = lax.rem(lax.axis_index(inner), 2) == 0
    half = lanes // 2
    keep = jnp.where(first, packed[:, :half], packed[:, half:])
    send = jnp.where(first, packed[:, half:], packed[:, :half])
    mine = keep + lax.ppermute(send, inner, pairs)
    chunk = -(-rows // (8 * outer_size)) * 8
    mine = jnp.pad(mine, ((0, chunk * outer_size - rows), (0, 0))).reshape(outer_size, chunk, half)
    total = jnp.sum(lax.all_to_all(mine, outer, 0, 0, tiled=True), axis=0)
    bit = 2
    while bit < inner_size:
        total = total + lax.ppermute(total, inner, [(i, i ^ bit) for i in range(inner_size)])
        bit *= 2
    total = lax.all_to_all(jnp.broadcast_to(total, (outer_size, chunk, half)), outer, 0, 0, tiled=True)
    mine = total.reshape(outer_size * chunk, half)[:rows]
    other = lax.ppermute(mine, inner, pairs)
    return jnp.where(first, jnp.concatenate([mine, other], axis=1), jnp.concatenate([other, mine], axis=1))


def gather_ring(block, axis, size):
    right = [(i, (i + 1) % size) for i in range(size)]
    left = [(i, (i - 1) % size) for i in range(size)]
    from_left = lax.ppermute(block, axis, right)
    from_right = lax.ppermute(block, axis, left)
    half = block.shape[0] // 2
    far_first = lax.ppermute(from_left[:half], axis, right)
    far_second = lax.ppermute(from_right[half:], axis, left)
    return jnp.concatenate([block, from_right, far_first, far_second, from_left], axis=0)


def rotate(chunks, shift, size):
    width = chunks.shape[-1]
    doubled = jnp.concatenate([chunks, chunks], axis=-1)
    start = ((size - shift) % size) * (width // size)
    return lax.dynamic_slice_in_dim(doubled, start, width, axis=chunks.ndim - 1)


def per_device(slab, vectors, tfactors):
    rows, cols = slab.shape
    count = tfactors.shape[0]
    width = tfactors.shape[1]
    ng = PCOL_PARTS[0] * PCOL_PARTS[1]
    nprow = PROW_SIZE

    ny = PCOL_PARTS[2]
    depth = vectors.shape[0]
    turn = lax.axis_index("y")
    basis = gather_ring(vectors, "y", ny)
    work = rotate(slab.reshape(rows, ng, ny * depth), -turn, ny).reshape(rows, cols)
    work = lax.all_to_all(work, GROUP, 1, 0, tiled=True)

    products = matmul(work, basis)
    grams = jnp.concatenate([matmul(basis[:, j * width : (j + 1) * width].T, basis[:, : j * width]) for j in range(1, count)], axis=1)
    lanes = products.shape[1]
    packed = jnp.concatenate([products, grams.reshape(-1, lanes)], axis=0)
    packed = all_reduce(packed, GROUP, "prow", ng, nprow)
    span = products.shape[0]
    grams = packed[span:].reshape(grams.shape)
    gram, offset = {}, 0
    for j in range(1, count):
        for k in range(j):
            gram[j, k], offset = grams[:, offset : offset + width], offset + width

    diagonal = jnp.zeros((count * width, count * width), tfactors.dtype)
    for k in range(count):
        diagonal = diagonal.at[k * width : (k + 1) * width, k * width : (k + 1) * width].set(tfactors[k].T)
    products = matmul(packed[:span], diagonal)
    scaled = [None] * count
    for k in reversed(range(count)):
        part = products[:, k * width : (k + 1) * width]
        if k + 1 < count:
            later = list(range(count - 1, k, -1))
            weights = matmul(jnp.concatenate([gram[j, k] for j in later], axis=0), tfactors[k].T)
            part = part - matmul(jnp.concatenate([scaled[j] for j in later], axis=1), weights)
        scaled[k] = part
    scaled = jnp.concatenate(scaled, axis=1)

    work = work - matmul(scaled, basis.T)
    work = lax.all_to_all(work, GROUP, 0, 1, tiled=True)
    return rotate(work.reshape(rows, ng, ny * depth), turn, ny).reshape(rows, cols)


def solution(mesh):
    devices = mesh.devices.reshape((mesh.shape["prow"],) + PCOL_PARTS)
    fine = Mesh(devices, ("prow", "x", "zl", "y"))
    cols = ("x", "zl", "y")
    in_specs = (P(cols, "prow"), P(("prow",) + cols, None), P())
    out_specs = P(cols, "prow")
    return jax.shard_map(per_device, mesh=fine, in_specs=in_specs, out_specs=out_specs, check_vma=False)
```

```python
import jax
import jax.numpy as jnp
from jax import lax
from jax.sharding import Mesh
from jax.sharding import PartitionSpec as P

PCOL_PARTS = (4, 2, 4)
GROUP = ("x", "zl")
PROW_SIZE = 8


def matmul(left, right):
    return jnp.dot(left, right, precision=lax.Precision.HIGH, preferred_element_type=jnp.float32)


def all_reduce(packed, outer, inner, outer_size, inner_size):
    rows, lanes = packed.shape
    pairs = [(i, i ^ 1) for i in range(inner_size)]
    first = lax.rem(lax.axis_index(inner), 2) == 0
    half = lanes // 2
    keep = jnp.where(first, packed[:, :half], packed[:, half:])
    send = jnp.where(first, packed[:, half:], packed[:, :half])
    mine = keep + lax.ppermute(send, inner, pairs)
    chunk = -(-rows // (8 * outer_size)) * 8
    mine = jnp.pad(mine, ((0, chunk * outer_size - rows), (0, 0))).reshape(outer_size, chunk, half)
    total = jnp.sum(lax.all_to_all(mine, outer, 0, 0, tiled=True), axis=0)
    peers = inner_size // 2
    terms = [total]
    for step in range(1, peers):
        terms.append(lax.ppermute(total, inner, [(i, ((i // 2 + step) % peers) * 2 + i % 2) for i in range(inner_size)]))
    total = sum(terms[1:], terms[0])
    total = lax.all_to_all(jnp.broadcast_to(total, (outer_size, chunk, half)), outer, 0, 0, tiled=True)
    mine = total.reshape(outer_size * chunk, half)[:rows]
    other = lax.ppermute(mine, inner, pairs)
    return jnp.where(first, jnp.concatenate([mine, other], axis=1), jnp.concatenate([other, mine], axis=1))


def gather_ring(block, axis, size):
    right = [(i, (i + 1) % size) for i in range(size)]
    left = [(i, (i - 1) % size) for i in range(size)]
    from_left = lax.ppermute(block, axis, right)
    from_right = lax.ppermute(block, axis, left)
    half = block.shape[0] // 2
    far_first = lax.ppermute(from_left[:half], axis, right)
    far_second = lax.ppermute(from_right[half:], axis, left)
    return jnp.concatenate([block, from_right, far_first, far_second, from_left], axis=0)


def rotate(chunks, shift, size):
    width = chunks.shape[-1]
    doubled = jnp.concatenate([chunks, chunks], axis=-1)
    start = ((size - shift) % size) * (width // size)
    return lax.dynamic_slice_in_dim(doubled, start, width, axis=chunks.ndim - 1)


def per_device(slab, vectors, tfactors):
    rows, cols = slab.shape
    count = tfactors.shape[0]
    width = tfactors.shape[1]
    ng = PCOL_PARTS[0] * PCOL_PARTS[1]
    nprow = PROW_SIZE

    ny = PCOL_PARTS[2]
    depth = vectors.shape[0]
    turn = lax.axis_index("y")
    basis = gather_ring(vectors, "y", ny)
    work = rotate(slab.reshape(rows, ng, ny * depth), -turn, ny).reshape(rows, cols)
    work = lax.all_to_all(work, GROUP, 1, 0, tiled=True)

    products = matmul(work, basis)
    grams = jnp.concatenate([matmul(basis[:, j * width : (j + 1) * width].T, basis[:, : j * width]) for j in range(1, count)], axis=1)
    lanes = products.shape[1]
    packed = jnp.concatenate([products, grams.reshape(-1, lanes)], axis=0)
    packed = all_reduce(packed, GROUP, "prow", ng, nprow)
    span = products.shape[0]
    grams = packed[span:].reshape(grams.shape)
    gram, offset = {}, 0
    for j in range(1, count):
        for k in range(j):
            gram[j, k], offset = grams[:, offset : offset + width], offset + width

    diagonal = jnp.zeros((count * width, count * width), tfactors.dtype)
    for k in range(count):
        diagonal = diagonal.at[k * width : (k + 1) * width, k * width : (k + 1) * width].set(tfactors[k].T)
    products = matmul(packed[:span], diagonal)
    scaled = [None] * count
    for k in reversed(range(count)):
        part = products[:, k * width : (k + 1) * width]
        if k + 1 < count:
            later = list(range(count - 1, k, -1))
            weights = matmul(jnp.concatenate([gram[j, k] for j in later], axis=0), tfactors[k].T)
            part = part - matmul(jnp.concatenate([scaled[j] for j in later], axis=1), weights)
        scaled[k] = part
    scaled = jnp.concatenate(scaled, axis=1)

    work = work - matmul(scaled, basis.T)
    work = lax.all_to_all(work, GROUP, 0, 1, tiled=True)
    return rotate(work.reshape(rows, ng, ny * depth), turn, ny).reshape(rows, cols)


def solution(mesh):
    devices = mesh.devices.reshape((mesh.shape["prow"],) + PCOL_PARTS)
    fine = Mesh(devices, ("prow", "x", "zl", "y"))
    cols = ("x", "zl", "y")
    in_specs = (P(cols, "prow"), P(("prow",) + cols, None), P())
    out_specs = P(cols, "prow")
    return jax.shard_map(per_device, mesh=fine, in_specs=in_specs, out_specs=out_specs, check_vma=False)
```

```python
import jax
import jax.numpy as jnp
from jax import lax
from jax.sharding import Mesh
from jax.sharding import PartitionSpec as P

PCOL_PARTS = (4, 2, 4)
GROUP = ("x", "zl")
PROW_SIZE = 8


def matmul(left, right):
    return jnp.dot(left, right, precision=lax.Precision.HIGH, preferred_element_type=jnp.float32)


def all_reduce(packed, outer, inner, outer_size, inner_size):
    rows, lanes = packed.shape
    pairs = [(i, i ^ 1) for i in range(inner_size)]
    first = lax.rem(lax.axis_index(inner), 2) == 0
    half = lanes // 2
    keep = jnp.where(first, packed[:, :half], packed[:, half:])
    send = jnp.where(first, packed[:, half:], packed[:, :half])
    mine = keep + lax.ppermute(send, inner, pairs)
    chunk = -(-rows // (8 * outer_size)) * 8
    mine = jnp.pad(mine, ((0, chunk * outer_size - rows), (0, 0))).reshape(outer_size, chunk, half)
    total = jnp.sum(lax.all_to_all(mine, outer, 0, 0, tiled=True), axis=0)
    bit = 2
    while bit < inner_size:
        total = total + lax.ppermute(total, inner, [(i, i ^ bit) for i in range(inner_size)])
        bit *= 2
    total = lax.all_to_all(jnp.broadcast_to(total, (outer_size, chunk, half)), outer, 0, 0, tiled=True)
    mine = total.reshape(outer_size * chunk, half)[:rows]
    other = lax.ppermute(mine, inner, pairs)
    return jnp.where(first, jnp.concatenate([mine, other], axis=1), jnp.concatenate([other, mine], axis=1))


def gather_ring(block, axis, size):
    right = [(i, (i + 1) % size) for i in range(size)]
    left = [(i, (i - 1) % size) for i in range(size)]
    from_left = lax.ppermute(block, axis, right)
    from_right = lax.ppermute(block, axis, left)
    half = block.shape[0] // 2
    far_first = lax.ppermute(from_left[:half], axis, right)
    far_second = lax.ppermute(from_right[half:], axis, left)
    return jnp.concatenate([block, from_right, far_first, far_second, from_left], axis=0)


def rotate(chunks, shift, size):
    width = chunks.shape[-1]
    doubled = jnp.concatenate([chunks, chunks], axis=-1)
    start = ((size - shift) % size) * (width // size)
    return lax.dynamic_slice_in_dim(doubled, start, width, axis=chunks.ndim - 1)


def per_device(slab, vectors, tfactors):
    rows, cols = slab.shape
    count = tfactors.shape[0]
    width = tfactors.shape[1]
    ng = PCOL_PARTS[0] * PCOL_PARTS[1]
    nprow = PROW_SIZE

    ny = PCOL_PARTS[2]
    depth = vectors.shape[0]
    turn = lax.axis_index("y")
    basis = gather_ring(vectors, "y", ny)
    work = rotate(slab.reshape(rows, ng, ny * depth), -turn, ny).reshape(rows, cols)
    work = lax.all_to_all(work, GROUP, 1, 0, tiled=True)

    products = matmul(work, basis)
    top = jnp.concatenate([matmul(basis[:, 3 * width : 4 * width].T, basis[:, : 3 * width]), matmul(basis[:, 2 * width : 3 * width].T, basis[:, width : 2 * width])], axis=1)
    low = matmul(jnp.concatenate([basis[:, 2 * width : 3 * width], basis[:, width : 2 * width]], axis=1).T, basis[:, :width])
    low = jnp.concatenate([low[:width], low[width:], jnp.zeros((width, 2 * width), low.dtype)], axis=1)
    packed = jnp.concatenate([products, top, low], axis=0)
    packed = all_reduce(packed, GROUP, "prow", ng, nprow)
    span = products.shape[0]
    top, low = packed[span : span + width], packed[span + width :]
    gram = {(3, 0): top[:, :width], (3, 1): top[:, width : 2 * width], (3, 2): top[:, 2 * width : 3 * width], (2, 1): top[:, 3 * width :],
            (2, 0): low[:, :width], (1, 0): low[:, width : 2 * width]}

    diagonal = jnp.zeros((count * width, count * width), tfactors.dtype)
    for k in range(count):
        diagonal = diagonal.at[k * width : (k + 1) * width, k * width : (k + 1) * width].set(tfactors[k].T)
    products = matmul(packed[:span], diagonal)
    scaled = [None] * count
    for k in reversed(range(count)):
        part = products[:, k * width : (k + 1) * width]
        if k + 1 < count:
            later = list(range(count - 1, k, -1))
            weights = matmul(jnp.concatenate([gram[j, k] for j in later], axis=0), tfactors[k].T)
            part = part - matmul(jnp.concatenate([scaled[j] for j in later], axis=1), weights)
        scaled[k] = part
    scaled = jnp.concatenate(scaled, axis=1)

    work = work - matmul(scaled, basis.T)
    work = lax.all_to_all(work, GROUP, 0, 1, tiled=True)
    return rotate(work.reshape(rows, ng, ny * depth), turn, ny).reshape(rows, cols)


def solution(mesh):
    devices = mesh.devices.reshape((mesh.shape["prow"],) + PCOL_PARTS)
    fine = Mesh(devices, ("prow", "x", "zl", "y"))
    cols = ("x", "zl", "y")
    in_specs = (P(cols, "prow"), P(("prow",) + cols, None), P())
    out_specs = P(cols, "prow")
    return jax.shard_map(per_device, mesh=fine, in_specs=in_specs, out_specs=out_specs, check_vma=False)
```
